512 devices in a mesh: ctx: 64 (over y_hi, x, z), head: 8 (over y_lo, core).
Axes of the slice: x: 4, y: 8 (y_hi: 2, y_lo: 4; y = y_hi * 4 + y_lo), z: 8, core: 2. Of those that a mesh axis runs over, the one named last changes fastest.
Arguments:
- q_self: bfloat16 [8192, 4096], P('ctx', 'head'), may hold values from -6 to 6
- k_self: bfloat16 [8192, 4096], P('ctx', 'head'), may hold values from -6 to 6
- v_self: bfloat16 [8192, 4096], P('ctx', 'head'), may hold values from -6 to 6
- q_cross: bfloat16 [8192, 4096], P('ctx', 'head'), may hold values from -6 to 6
- n_keys: bfloat16 [32768, 4096], P('ctx', 'head'), may hold values from -6 to 6
- n_values: bfloat16 [32768, 4096], P('ctx', 'head'), may hold values from -6 to 6
- d_cross: bfloat16 [8192, 4096], P('ctx', 'head'), may hold values from -16 to 16
Outputs:
- self_out: bfloat16 [8192, 4096], P('ctx', 'head')
- cross_out: bfloat16 [8192, 4096], P('ctx', 'head')
- d_query: bfloat16 [8192, 4096], P('ctx', 'head')
- d_keys: bfloat16 [32768, 4096], P('ctx', 'head')
- d_values: bfloat16 [32768, 4096], P('ctx', 'head')
The draws below stay inside these ranges and needn't reach their ends.
All inputs are finite; a program needn't handle non-finite values.
Results may differ from the reference program's by a relative error of at most 0.012.
Values may be sent and summed in bfloat16 or wider, within the bound.
No kernel may reach another device: no remote copies, remote signals or barrier semaphores. Data moves between devices by JAX's collectives and lax.ppermute only.
A program may use at most 128 MiB of HBM per device.

```python
import math
import jax
import jax.numpy as jnp
from jax import lax

HD = 128
SPAN = 64
COLS = 4096
TOKENS = 8192
NROWS = 32768


def base_values(key, offset_tag, row_count):
    folded = jax.random.fold_in(key, offset_tag)
    return jnp.clip(jax.random.normal(folded, (row_count, COLS), jnp.float32), -4.5, 4.5)


def drawn_queries(key, offset_tag, row_count):
    values_drawn = base_values(key, offset_tag, row_count)
    return values_drawn.astype(jnp.bfloat16)


def drawn_keys(key, offset_tag, row_count):
    values_drawn = base_values(key, offset_tag, row_count)
    return values_drawn.astype(jnp.bfloat16)


def draw_q_self(key, part):
    return drawn_queries(key, 100, TOKENS)


def draw_k_self(key, part):
    return drawn_keys(key, 200, TOKENS)


def draw_q_cross(key, part):
    return drawn_queries(key, 300, TOKENS)


def draw_n_keys(key, part):
    return drawn_keys(key, 400, NROWS)


def draw_d_cross(key, part):
    folded = jax.random.fold_in(key, 500)
    position = jnp.arange(TOKENS, dtype=jnp.float32) / TOKENS
    values_drawn = jnp.clip(jax.random.normal(folded, (TOKENS, COLS), jnp.float32), -4.0, 4.0)
    rising = 1.0 + 2.0 * position
    return (values_drawn * rising[:, None]).astype(jnp.bfloat16)


def shard_levels(own_key, extent, split, least, largest):
    loudness, own = 1.0, jax.random.fold_in(own_key, 6)
    for dim, shards_of in split:
        draws = jnp.exp(jax.random.uniform(jax.random.fold_in(own, dim), (shards_of,), jnp.float32, least / len(split), largest / len(split)))
        loudness = loudness * jnp.repeat(draws, extent[dim] // shards_of).reshape([-1 if axis == dim else 1 for axis in range(len(extent))])
    return loudness


def scatter_about(rng, extent, width, reach, pieces=(), kind=jnp.bfloat16):
    drawn = width * jax.random.normal(rng, extent, jnp.float32)
    if pieces:
        drawn = drawn * shard_levels(rng, extent, pieces, -0.22, 0.18)
    return jnp.clip(drawn, -reach, reach).astype(kind)


def setup_inputs(seed: int = 0) -> dict:
    seeds = jax.random.split(jax.random.key(seed), 8)
    return {
        "q_self": draw_q_self(jax.random.fold_in(seeds[7], 71), 0),
        "k_self": draw_k_self(jax.random.fold_in(seeds[7], 71), 0),
        "v_self": scatter_about(seeds[2], (TOKENS, COLS), 1.0, 6.0, ((0, 64), (1, 8))),
        "q_cross": draw_q_cross(jax.random.fold_in(seeds[7], 71), 0),
        "n_keys": draw_n_keys(jax.random.fold_in(seeds[7], 71), 0),
        "n_values": scatter_about(seeds[5], (NROWS, COLS), 1.0, 6.0, ((0, 64), (1, 8))),
        "d_cross": draw_d_cross(jax.random.fold_in(seeds[7], 71), 0),
    }


def causal_block(query_rows, first_position, keys_head, values_head):
    scale_factor = 1.0 / math.sqrt(keys_head.shape[1])
    scores = jnp.dot(query_rows, keys_head.T, preferred_element_type=jnp.float32) * scale_factor
    positions = first_position + jnp.arange(query_rows.shape[0], dtype=jnp.int32)
    key_positions = jnp.arange(keys_head.shape[0], dtype=jnp.int32)
    visible = key_positions[None, :] <= positions[:, None]
    masked = jnp.where(visible, scores, jnp.float32(-1e+30))
    row_max = lax.optimization_barrier(jnp.max(masked, axis=1, keepdims=True))
    weights = jnp.where(visible, jnp.exp(masked - row_max), jnp.float32(0.0))
    row_total = lax.optimization_barrier(jnp.sum(weights, axis=1, keepdims=True))
    mixed = jnp.dot(weights.astype(jnp.bfloat16), values_head, preferred_element_type=jnp.float32)
    return (mixed / row_total).astype(jnp.bfloat16)

def self_attention(q_self, k_self, v_self):
    token_count, column_count = q_self.shape
    head_count = column_count // HD
    block_rows = min(512, token_count)
    block_count = token_count // block_rows

    def by_heads(array):
        return array.reshape(token_count, head_count, HD).transpose(1, 0, 2)

    def per_head(operands):
        query_head, keys_head, values_head = operands
        query_blocks = query_head.reshape(block_count, block_rows, HD)
        firsts = jnp.arange(block_count, dtype=jnp.int32) * block_rows

        def per_block(items):
            return causal_block(items[0], items[1], keys_head, values_head)
        return lax.map(per_block, (query_blocks, firsts)).reshape(token_count, HD)
    result = lax.map(per_head, (by_heads(q_self), by_heads(k_self), by_heads(v_self)))
    return result.transpose(1, 0, 2).reshape(token_count, column_count)

def cross_span(operands):
    query_rows, keys_rows, values_rows, grad_rows = operands
    row_count, column_count = query_rows.shape
    head_count = column_count // HD
    neighbour_count = keys_rows.shape[0]
    scale_factor = 1.0 / math.sqrt(HD)
    queries = query_rows.reshape(row_count, head_count, HD).astype(jnp.float32)
    keys_four = keys_rows.reshape(neighbour_count, head_count, HD).astype(jnp.float32)
    values_four = values_rows.reshape(neighbour_count, head_count, HD).astype(jnp.float32)
    grads_four = grad_rows.reshape(row_count, head_count, HD).astype(jnp.float32)
    scores = jnp.einsum('rhd,khd->hrk', queries, keys_four) * scale_factor
    row_max = lax.optimization_barrier(jnp.max(scores, axis=2, keepdims=True))
    weights = jnp.exp(scores - row_max)
    probs = weights / lax.optimization_barrier(jnp.sum(weights, axis=2, keepdims=True))
    probs_low = probs.astype(jnp.bfloat16)
    attended = jnp.einsum('hrk,khd->rhd', probs_low.astype(jnp.float32), values_four)
    grad_probs = jnp.einsum('rhd,khd->hrk', grads_four, values_four)
    centre = lax.optimization_barrier(jnp.sum(grad_probs * probs, axis=2, keepdims=True))
    grad_scores = (probs * (grad_probs - centre) * scale_factor).astype(jnp.bfloat16)
    grad_query = jnp.einsum('hrk,khd->rhd', grad_scores.astype(jnp.float32), keys_four)
    grad_keys = jnp.einsum('hrk,rhd->khd', grad_scores.astype(jnp.float32), queries)
    grad_values = jnp.einsum('hrk,rhd->khd', probs_low.astype(jnp.float32), grads_four)
    return (attended.reshape(row_count, column_count).astype(jnp.bfloat16), grad_query.reshape(row_count, column_count).astype(jnp.bfloat16), grad_keys.reshape(neighbour_count, column_count), grad_values.reshape(neighbour_count, column_count))

def reference(q_self, k_self, v_self, q_cross, n_keys, n_values, d_cross):
    self_out = self_attention(q_self, k_self, v_self)
    token_count, column_count = q_cross.shape
    lag_rows = SPAN - 1
    shifted = jnp.concatenate([q_cross[lag_rows:], jnp.zeros((lag_rows, column_count), jnp.bfloat16)], axis=0)
    span_count = token_count // SPAN
    neighbour_rows = n_keys.shape[0] // span_count
    results = lax.map(cross_span, (shifted.reshape(span_count, SPAN, column_count), n_keys.reshape(span_count, neighbour_rows, column_count), n_values.reshape(span_count, neighbour_rows, column_count), d_cross.reshape(span_count, SPAN, column_count)))
    cross_out = results[0].reshape(token_count, column_count)
    grad_source = results[1].reshape(token_count, column_count)
    d_query = jnp.concatenate([jnp.zeros((lag_rows, column_count), jnp.bfloat16), grad_source[:token_count - lag_rows]], axis=0)
    grad_keys = results[2]
    grad_values = results[3]
    mean_square = (jnp.sum(grad_keys * grad_keys) + jnp.sum(grad_values * grad_values)) / (2.0 * grad_keys.size)
    factor = lax.rsqrt(mean_square + 1e-06)
    d_keys = (grad_keys * factor).astype(jnp.bfloat16).reshape(n_keys.shape)
    d_values = (grad_values * factor).astype(jnp.bfloat16).reshape(n_values.shape)
    return (self_out, cross_out, d_query, d_keys, d_values)
```

```python
import math

import jax
import jax.numpy as jnp
from jax import lax
from jax.sharding import Mesh
from jax.sharding import PartitionSpec as P

HD = 128
SPAN = 64
CTX = ("outer", "z")


def from_behind(block, count, distance):
    route = [(i - distance, i) for i in range(count) if 0 <= i - distance < count]
    return lax.ppermute(block, CTX, route)


def spread(block, axis, count):
    copies = jnp.broadcast_to(block[None], (count,) + block.shape)
    return lax.all_to_all(copies, axis, 0, 0, tiled=True)


def self_attention(q_self, k_self, v_self, outer_count, z_count):
    row_count, column_count = q_self.shape
    head_count = column_count // HD
    outer_index = lax.axis_index("outer")
    z_index = lax.axis_index("z")
    pair = jnp.concatenate([k_self, v_self], axis=1)
    group = spread(pair, "z", z_count).reshape(z_count * row_count, 2 * column_count)
    keys = group[:, :column_count].reshape(z_count * row_count, head_count, HD)
    values = group[:, column_count:].reshape(z_count * row_count, head_count, HD)
    queries = spread(q_self, "outer", outer_count).reshape(outer_count, row_count, head_count, HD)
    key_first = outer_index * z_count * row_count
    key_positions = key_first + jnp.arange(z_count * row_count, dtype=jnp.int32)
    query_starts = (jnp.arange(outer_count, dtype=jnp.int32) * z_count + z_index) * row_count
    query_positions = query_starts[:, None] + jnp.arange(row_count, dtype=jnp.int32)[None, :]
    visible = (key_positions[None, None, :] <= query_positions[:, :, None])[None]
    scores = jnp.einsum("grhd,khd->hgrk", queries, keys, preferred_element_type=jnp.float32) * (
        1.0 / math.sqrt(HD)
    )
    masked = jnp.where(visible, scores, jnp.float32(-1e30))
    part_max = jnp.max(masked, axis=3)
    weights = jnp.where(visible, jnp.exp(masked - part_max[..., None]), jnp.float32(0.0))
    part_sum = jnp.sum(weights, axis=3)
    part_acc = jnp.einsum(
        "hgrk,khd->grhd", weights.astype(jnp.bfloat16), values, preferred_element_type=jnp.float32
    ).reshape(outer_count, row_count, column_count)
    stats = jnp.concatenate(
        [part_max.transpose(1, 2, 0), part_sum.transpose(1, 2, 0)], axis=2
    )
    packed = jnp.concatenate([part_acc, stats], axis=2)
    back = lax.all_to_all(packed, "outer", 0, 0, tiled=True)
    got_acc = back[:, :, :column_count].reshape(outer_count, row_count, head_count, HD)
    got_max = back[:, :, column_count : column_count + head_count]
    got_sum = back[:, :, column_count + head_count :]
    top = jnp.max(got_max, axis=0)
    rescale = jnp.exp(got_max - top[None])
    total = jnp.sum(got_sum * rescale, axis=0)
    mixed = jnp.sum(got_acc * rescale[..., None], axis=0)
    out = mixed / total[..., None]
    return out.reshape(row_count, column_count).astype(jnp.bfloat16)


def cross_attention(q_cross, n_keys, n_values, d_cross, ctx_count, element_total):
    row_count, column_count = q_cross.shape
    head_count = column_count // HD
    lag_rows = SPAN - 1
    scale_factor = 1.0 / math.sqrt(HD)
    incoming = from_behind(q_cross[:lag_rows], ctx_count, -1)
    shifted = jnp.concatenate([q_cross[lag_rows:], incoming], axis=0)
    span_count = row_count // SPAN
    neighbour_rows = n_keys.shape[0] // span_count
    queries = shifted.reshape(span_count, SPAN, head_count, HD)
    neighbour_keys = n_keys.reshape(span_count, neighbour_rows, head_count, HD)
    neighbour_values = n_values.reshape(span_count, neighbour_rows, head_count, HD)
    grad_rows = d_cross.reshape(span_count, SPAN, head_count, HD)
    scores = (
        jnp.einsum("crhd,ckhd->chrk", queries, neighbour_keys, preferred_element_type=jnp.float32)
        * scale_factor
    )
    row_max = jnp.max(scores, axis=3, keepdims=True)
    weights = jnp.exp(scores - row_max)
    probs = weights / jnp.sum(weights, axis=3, keepdims=True)
    probs_low = probs.astype(jnp.bfloat16)
    attended = jnp.einsum(
        "chrk,ckhd->crhd", probs_low, neighbour_values, preferred_element_type=jnp.float32
    )
    cross_out = attended.reshape(row_count, column_count).astype(jnp.bfloat16)
    grad_probs = jnp.einsum(
        "crhd,ckhd->chrk", grad_rows, neighbour_values, preferred_element_type=jnp.float32
    )
    centre = jnp.sum(grad_probs * probs, axis=3, keepdims=True)
    grad_scores = (probs * (grad_probs - centre) * scale_factor).astype(jnp.bfloat16)
    grad_source = jnp.einsum(
        "chrk,ckhd->crhd", grad_scores, neighbour_keys, preferred_element_type=jnp.float32
    )
    grad_source = grad_source.reshape(row_count, column_count).astype(jnp.bfloat16)
    grad_keys = jnp.einsum(
        "chrk,crhd->ckhd", grad_scores, queries, preferred_element_type=jnp.float32
    ).reshape(n_keys.shape)
    grad_values = jnp.einsum(
        "chrk,crhd->ckhd", probs_low, grad_rows, preferred_element_type=jnp.float32
    ).reshape(n_values.shape)
    carried = from_behind(grad_source[row_count - lag_rows :], ctx_count, 1)
    d_query = jnp.concatenate([carried, grad_source[: row_count - lag_rows]], axis=0)
    squares = jnp.sum(grad_keys * grad_keys) + jnp.sum(grad_values * grad_values)
    overall = lax.psum(squares, ("outer", "z", "head"))
    factor = lax.rsqrt(overall / element_total + 1e-06)
    d_keys = (grad_keys * factor).astype(jnp.bfloat16)
    d_values = (grad_values * factor).astype(jnp.bfloat16)
    return (cross_out, d_query, d_keys, d_values)


def solution(mesh):
    outer_count = mesh.shape["ctx"] // 8
    z_count = 8
    head_count = mesh.shape["head"]
    regrouped = Mesh(
        mesh.devices.reshape(outer_count, z_count, head_count), ("outer", "z", "head")
    )
    ctx_count = outer_count * z_count

    def body(q_self, k_self, v_self, q_cross, n_keys, n_values, d_cross):
        element_total = 2.0 * n_keys.size * ctx_count * head_count
        self_out = self_attention(q_self, k_self, v_self, outer_count, z_count)
        cross_out, d_query, d_keys, d_values = cross_attention(
            q_cross, n_keys, n_values, d_cross, ctx_count, element_total
        )
        return (self_out, cross_out, d_query, d_keys, d_values)

    spec = P(CTX, "head")
    return jax.shard_map(
        body, mesh=regrouped, in_specs=(spec,) * 7, out_specs=(spec,) * 5, check_vma=False
    )
```

```python
import math

import jax
import jax.numpy as jnp
from jax import lax
from jax.sharding import Mesh
from jax.sharding import PartitionSpec as P

HD = 128
SPAN = 64
CTX = ("outer", "z")


def from_behind(block, count, distance):
    route = [(i - distance, i) for i in range(count) if 0 <= i - distance < count]
    return lax.ppermute(block, CTX, route)


def spread(block, axis, count):
    copies = jnp.broadcast_to(block[None], (count,) + block.shape)
    return lax.all_to_all(copies, axis, 0, 0, tiled=True)


def self_attention(q_self, k_self, v_self, outer_count, z_count):
    row_count, column_count = q_self.shape
    head_count = column_count // HD
    outer_index = lax.axis_index("outer")
    z_index = lax.axis_index("z")
    pair = jnp.concatenate([k_self, v_self], axis=1)
    group = spread(pair, "z", z_count).reshape(z_count * row_count, 2 * column_count)
    keys = group[:, :column_count].reshape(z_count * row_count, head_count, HD)
    values = group[:, column_count:].reshape(z_count * row_count, head_count, HD)
    queries = spread(q_self, "outer", outer_count).reshape(outer_count, row_count, head_count, HD)
    key_first = outer_index * z_count * row_count
    key_positions = key_first + jnp.arange(z_count * row_count, dtype=jnp.int32)
    query_starts = (jnp.arange(outer_count, dtype=jnp.int32) * z_count + z_index) * row_count
    query_positions = query_starts[:, None] + jnp.arange(row_count, dtype=jnp.int32)[None, :]
    visible = (key_positions[None, None, :] <= query_positions[:, :, None])[None]
    scores = jnp.einsum("grhd,khd->hgrk", queries, keys, preferred_element_type=jnp.float32) * (
        1.0 / math.sqrt(HD)
    )
    masked = jnp.where(visible, scores, jnp.float32(-1e30))
    part_max = jnp.max(masked, axis=3)
    weights = jnp.where(visible, jnp.exp(masked - part_max[..., None]), jnp.float32(0.0))
    part_sum = jnp.sum(weights, axis=3)
    part_acc = jnp.einsum(
        "hgrk,khd->grhd", weights.astype(jnp.bfloat16), values, preferred_element_type=jnp.float32
    ).reshape(outer_count, row_count, column_count)
    stats = jnp.concatenate(
        [part_max.transpose(1, 2, 0), part_sum.transpose(1, 2, 0)], axis=2
    )
    packed = jnp.concatenate([part_acc, stats], axis=2)
    back = lax.all_to_all(packed, "outer", 0, 0, tiled=True)
    got_acc = back[:, :, :column_count].reshape(outer_count, row_count, head_count, HD)
    got_max = back[:, :, column_count : column_count + head_count]
    got_sum = back[:, :, column_count + head_count :]
    top = jnp.max(got_max, axis=0)
    rescale = jnp.exp(got_max - top[None])
    total = jnp.sum(got_sum * rescale, axis=0)
    mixed = jnp.sum(got_acc * rescale[..., None], axis=0)
    out = mixed / total[..., None]
    return out.reshape(row_count, column_count).astype(jnp.bfloat16)


def cross_attention(q_cross, n_keys, n_values, d_cross, ctx_count, element_total):
    row_count, column_count = q_cross.shape
    head_count = column_count // HD
    lag_rows = SPAN - 1
    scale_factor = 1.0 / math.sqrt(HD)
    incoming = from_behind(q_cross[:lag_rows], ctx_count, -1)
    shifted = jnp.concatenate([q_cross[lag_rows:], incoming], axis=0)
    span_count = row_count // SPAN
    neighbour_rows = n_keys.shape[0] // span_count
    queries = shifted.reshape(span_count, SPAN, head_count, HD)
    neighbour_keys = n_keys.reshape(span_count, neighbour_rows, head_count, HD)
    neighbour_values = n_values.reshape(span_count, neighbour_rows, head_count, HD)
    grad_rows = d_cross.reshape(span_count, SPAN, head_count, HD)
    scores = (
        jnp.einsum("crhd,ckhd->chrk", queries, neighbour_keys, preferred_element_type=jnp.float32)
        * scale_factor
    )
    row_max = jnp.max(scores, axis=3, keepdims=True)
    weights = jnp.exp(scores - row_max)
    probs = weights / jnp.sum(weights, axis=3, keepdims=True)
    probs_low = probs.astype(jnp.bfloat16)
    attended = jnp.einsum(
        "chrk,ckhd->crhd", probs_low, neighbour_values, preferred_element_type=jnp.float32
    )
    cross_out = attended.reshape(row_count, column_count).astype(jnp.bfloat16)
    grad_probs = jnp.einsum(
        "crhd,ckhd->chrk", grad_rows, neighbour_values, preferred_element_type=jnp.float32
    )
    centre = jnp.sum(grad_probs * probs, axis=3, keepdims=True)
    grad_scores = (probs * (grad_probs - centre) * scale_factor).astype(jnp.bfloat16)
    grad_source = jnp.einsum(
        "chrk,ckhd->crhd", grad_scores, neighbour_keys, preferred_element_type=jnp.float32
    )
    grad_source = grad_source.reshape(row_count, column_count).astype(jnp.bfloat16)
    grad_keys = jnp.einsum(
        "chrk,crhd->ckhd", grad_scores, queries, preferred_element_type=jnp.float32
    ).reshape(n_keys.shape)
    grad_values = jnp.einsum(
        "chrk,crhd->ckhd", probs_low, grad_rows, preferred_element_type=jnp.float32
    ).reshape(n_values.shape)
    carried = from_behind(grad_source[row_count - lag_rows :], ctx_count, 1)
    d_query = jnp.concatenate([carried, grad_source[: row_count - lag_rows]], axis=0)
    squares = jnp.sum(grad_keys * grad_keys) + jnp.sum(grad_values * grad_values)
    device_count = ctx_count * lax.axis_size("head")
    every = lax.all_to_all(
        jnp.broadcast_to(squares[None], (device_count,)), ("outer", "z", "head"), 0, 0, tiled=True
    )
    overall = jnp.sum(every)
    factor = lax.rsqrt(overall / element_total + 1e-06)
    d_keys = (grad_keys * factor).astype(jnp.bfloat16)
    d_values = (grad_values * factor).astype(jnp.bfloat16)
    return (cross_out, d_query, d_keys, d_values)


def solution(mesh):
    outer_count = mesh.shape["ctx"] // 8
    z_count = 8
    head_count = mesh.shape["head"]
    regrouped = Mesh(
        mesh.devices.reshape(outer_count, z_count, head_count), ("outer", "z", "head")
    )
    ctx_count = outer_count * z_count

    def body(q_self, k_self, v_self, q_cross, n_keys, n_values, d_cross):
        element_total = 2.0 * n_keys.size * ctx_count * head_count
        self_out = self_attention(q_self, k_self, v_self, outer_count, z_count)
        cross_out, d_query, d_keys, d_values = cross_attention(
            q_cross, n_keys, n_values, d_cross, ctx_count, element_total
        )
        return (self_out, cross_out, d_query, d_keys, d_values)

    spec = P(CTX, "head")
    return jax.shard_map(
        body, mesh=regrouped, in_specs=(spec,) * 7, out_specs=(spec,) * 5, check_vma=False
    )
```

```python
import math

import jax
import jax.numpy as jnp
from jax import lax
from jax.sharding import Mesh
from jax.sharding import PartitionSpec as P

HD = 128
SPAN = 64
CTX = ("outer", "z")


def from_behind(block, count, distance):
    route = [(i - distance, i) for i in range(count) if 0 <= i - distance < count]
    return lax.ppermute(block, CTX, route)


def spread(block, axis, count):
    copies = jnp.broadcast_to(block[None], (count,) + block.shape)
    return lax.all_to_all(copies, axis, 0, 0, tiled=True)


def self_attention(q_self, k_self, v_self, outer_count, z_count):
    row_count, column_count = q_self.shape
    head_count = column_count // HD
    outer_index = lax.axis_index("outer")
    z_index = lax.axis_index("z")
    pair = jnp.concatenate([k_self, v_self], axis=1)
    group = spread(pair, "z", z_count).reshape(z_count * row_count, 2 * column_count)
    keys = group[:, :column_count].reshape(z_count * row_count, head_count, HD)
    values = group[:, column_count:].reshape(z_count * row_count, head_count, HD)
    queries = spread(q_self, "outer", outer_count).reshape(outer_count, row_count, head_count, HD)
    key_first = outer_index * z_count * row_count
    key_positions = key_first + jnp.arange(z_count * row_count, dtype=jnp.int32)
    query_starts = (jnp.arange(outer_count, dtype=jnp.int32) * z_count + z_index) * row_count
    query_positions = query_starts[:, None] + jnp.arange(row_count, dtype=jnp.int32)[None, :]
    visible = (key_positions[None, None, :] <= query_positions[:, :, None])[None]
    scores = jnp.einsum("grhd,khd->hgrk", queries, keys, preferred_element_type=jnp.float32) * (
        1.0 / math.sqrt(HD)
    )
    masked = jnp.where(visible, scores, jnp.float32(-1e30))
    part_max = jnp.max(masked, axis=3)
    weights = jnp.where(visible, jnp.exp(masked - part_max[..., None]), jnp.float32(0.0))
    part_sum = jnp.sum(weights, axis=3)
    part_acc = jnp.einsum(
        "hgrk,khd->grhd", weights.astype(jnp.bfloat16), values, preferred_element_type=jnp.float32
    )
    present = part_sum > 0
    inverse = jnp.where(present, 1.0 / jnp.where(present, part_sum, 1.0), 0.0)
    part_out = (part_acc * inverse.transpose(1, 2, 0)[..., None]).astype(jnp.bfloat16)
    level = jnp.where(present, part_max + jnp.log(jnp.where(present, part_sum, 1.0)), -1e30)
    level = level.transpose(1, 2, 0)
    pieces = []
    rest = level
    for unused in range(3):
        piece = lax.optimization_barrier(rest.astype(jnp.bfloat16))
        pieces.append(piece)
        rest = rest - piece.astype(jnp.float32)
    packed = jnp.concatenate(
        [part_out.reshape(outer_count, row_count, column_count)] + pieces, axis=2
    )
    back = lax.all_to_all(packed, "outer", 0, 0, tiled=True)
    got_out = back[:, :, :column_count].reshape(outer_count, row_count, head_count, HD)
    got_level = sum(
        back[:, :, column_count + i * head_count : column_count + (i + 1) * head_count].astype(
            jnp.float32
        )
        for i in range(3)
    )
    top = jnp.max(got_level, axis=0)
    rescale = jnp.exp(got_level - top[None])
    total = jnp.sum(rescale, axis=0)
    mixed = jnp.sum(got_out.astype(jnp.float32) * rescale[..., None], axis=0)
    out = mixed / total[..., None]
    return out.reshape(row_count, column_count).astype(jnp.bfloat16)


def cross_attention(q_cross, n_keys, n_values, d_cross, ctx_count, element_total):
    row_count, column_count = q_cross.shape
    head_count = column_count // HD
    lag_rows = SPAN - 1
    scale_factor = 1.0 / math.sqrt(HD)
    incoming = from_behind(q_cross[:lag_rows], ctx_count, -1)
    shifted = jnp.concatenate([q_cross[lag_rows:], incoming], axis=0)
    span_count = row_count // SPAN
    neighbour_rows = n_keys.shape[0] // span_count
    queries = shifted.reshape(span_count, SPAN, head_count, HD)
    neighbour_keys = n_keys.reshape(span_count, neighbour_rows, head_count, HD)
    neighbour_values = n_values.reshape(span_count, neighbour_rows, head_count, HD)
    grad_rows = d_cross.reshape(span_count, SPAN, head_count, HD)
    scores = (
        jnp.einsum("crhd,ckhd->chrk", queries, neighbour_keys, preferred_element_type=jnp.float32)
        * scale_factor
    )
    row_max = jnp.max(scores, axis=3, keepdims=True)
    weights = jnp.exp(scores - row_max)
    probs = weights / jnp.sum(weights, axis=3, keepdims=True)
    probs_low = probs.astype(jnp.bfloat16)
    attended = jnp.einsum(
        "chrk,ckhd->crhd", probs_low, neighbour_values, preferred_element_type=jnp.float32
    )
    cross_out = attended.reshape(row_count, column_count).astype(jnp.bfloat16)
    grad_probs = jnp.einsum(
        "crhd,ckhd->chrk", grad_rows, neighbour_values, preferred_element_type=jnp.float32
    )
    centre = jnp.sum(grad_probs * probs, axis=3, keepdims=True)
    grad_scores = (probs * (grad_probs - centre) * scale_factor).astype(jnp.bfloat16)
    grad_source = jnp.einsum(
        "chrk,ckhd->crhd", grad_scores, neighbour_keys, preferred_element_type=jnp.float32
    )
    grad_source = grad_source.reshape(row_count, column_count).astype(jnp.bfloat16)
    grad_keys = jnp.einsum(
        "chrk,crhd->ckhd", grad_scores, queries, preferred_element_type=jnp.float32
    ).reshape(n_keys.shape)
    grad_values = jnp.einsum(
        "chrk,crhd->ckhd", probs_low, grad_rows, preferred_element_type=jnp.float32
    ).reshape(n_values.shape)
    carried = from_behind(grad_source[row_count - lag_rows :], ctx_count, 1)
    d_query = jnp.concatenate([carried, grad_source[: row_count - lag_rows]], axis=0)
    squares = jnp.sum(grad_keys * grad_keys) + jnp.sum(grad_values * grad_values)
    device_count = ctx_count * lax.axis_size("head")
    every = lax.all_to_all(
        jnp.broadcast_to(squares[None], (device_count,)), ("outer", "z", "head"), 0, 0, tiled=True
    )
    overall = jnp.sum(every)
    factor = lax.rsqrt(overall / element_total + 1e-06)
    d_keys = (grad_keys * factor).astype(jnp.bfloat16)
    d_values = (grad_values * factor).astype(jnp.bfloat16)
    return (cross_out, d_query, d_keys, d_values)


def solution(mesh):
    outer_count = mesh.shape["ctx"] // 8
    z_count = 8
    head_count = mesh.shape["head"]
    regrouped = Mesh(
        mesh.devices.reshape(outer_count, z_count, head_count), ("outer", "z", "head")
    )
    ctx_count = outer_count * z_count

    def body(q_self, k_self, v_self, q_cross, n_keys, n_values, d_cross):
        element_total = 2.0 * n_keys.size * ctx_count * head_count
        self_out = self_attention(q_self, k_self, v_self, outer_count, z_count)
        cross_out, d_query, d_keys, d_values = cross_attention(
            q_cross, n_keys, n_values, d_cross, ctx_count, element_total
        )
        return (self_out, cross_out, d_query, d_keys, d_values)

    spec = P(CTX, "head")
    return jax.shard_map(
        body, mesh=regrouped, in_specs=(spec,) * 7, out_specs=(spec,) * 5, check_vma=False
    )
```

```python
import math

import jax
import jax.numpy as jnp
from jax import lax
from jax.sharding import Mesh
from jax.sharding import PartitionSpec as P

HD = 128
SPAN = 64
CTX = ("outer", "z")


def from_behind(block, count, distance):
    route = [(i - distance, i) for i in range(count) if 0 <= i - distance < count]
    return lax.ppermute(block, CTX, route)


def spread(block, axis, count):
    copies = jnp.broadcast_to(block[None], (count,) + block.shape)
    return lax.all_to_all(copies, axis, 0, 0, tiled=True)


def self_attention(q_self, k_self, v_self, outer_count, z_count):
    row_count, column_count = q_self.shape
    head_count = column_count // HD
    outer_index = lax.axis_index("outer")
    z_index = lax.axis_index("z")
    pair = jnp.concatenate([k_self, v_self], axis=1)
    group = spread(pair, "z", z_count).reshape(z_count * row_count, 2 * column_count)
    keys = group[:, :column_count].reshape(z_count * row_count, head_count, HD)
    values = group[:, column_count:].reshape(z_count * row_count, head_count, HD)
    queries = spread(q_self, "outer", outer_count).reshape(outer_count, row_count, head_count, HD)
    key_first = outer_index * z_count * row_count
    key_positions = key_first + jnp.arange(z_count * row_count, dtype=jnp.int32)
    query_starts = (jnp.arange(outer_count, dtype=jnp.int32) * z_count + z_index) * row_count
    query_positions = query_starts[:, None] + jnp.arange(row_count, dtype=jnp.int32)[None, :]
    visible = (key_positions[None, None, :] <= query_positions[:, :, None])[None]
    scores = jnp.einsum("grhd,khd->hgrk", queries, keys, preferred_element_type=jnp.float32) * (
        1.0 / math.sqrt(HD)
    )
    masked = jnp.where(visible, scores, jnp.float32(-1e30))
    part_max = jnp.max(masked, axis=3)
    weights = jnp.where(visible, jnp.exp(masked - part_max[..., None]), jnp.float32(0.0))
    part_sum = jnp.sum(weights, axis=3)
    part_acc = jnp.einsum(
        "hgrk,khd->grhd", weights.astype(jnp.bfloat16), values, preferred_element_type=jnp.float32
    )
    present = part_sum > 0
    inverse = jnp.where(present, 1.0 / jnp.where(present, part_sum, 1.0), 0.0)
    part_out = (part_acc * inverse.transpose(1, 2, 0)[..., None]).astype(jnp.bfloat16)
    level = jnp.where(present, part_max + jnp.log(jnp.where(present, part_sum, 1.0)), -1e30)
    level = level.transpose(1, 2, 0)
    pieces = []
    rest = level
    for unused in range(3):
        piece = lax.optimization_barrier(rest.astype(jnp.bfloat16))
        pieces.append(piece)
        rest = rest - piece.astype(jnp.float32)
    packed = jnp.concatenate(
        [part_out.reshape(outer_count, row_count, column_count)] + pieces, axis=2
    )
    back = lax.all_to_all(packed, "outer", 0, 0, tiled=True)
    got_out = back[:, :, :column_count].reshape(outer_count, row_count, head_count, HD)
    got_level = sum(
        back[:, :, column_count + i * head_count : column_count + (i + 1) * head_count].astype(
            jnp.float32
        )
        for i in range(3)
    )
    top = jnp.max(got_level, axis=0)
    rescale = jnp.exp(got_level - top[None])
    total = jnp.sum(rescale, axis=0)
    mixed = jnp.sum(got_out.astype(jnp.float32) * rescale[..., None], axis=0)
    out = mixed / total[..., None]
    return out.reshape(row_count, column_count).astype(jnp.bfloat16)


def cross_attention(q_cross, n_keys, n_values, d_cross, ctx_count, element_total):
    row_count, column_count = q_cross.shape
    head_count = column_count // HD
    lag_rows = SPAN - 1
    scale_factor = 1.0 / math.sqrt(HD)
    incoming = from_behind(q_cross[:lag_rows], ctx_count, -1)
    shifted = jnp.concatenate([q_cross[lag_rows:], incoming], axis=0)
    span_count = row_count // SPAN
    neighbour_rows = n_keys.shape[0] // span_count
    queries = shifted.reshape(span_count, SPAN, head_count, HD)
    neighbour_keys = n_keys.reshape(span_count, neighbour_rows, head_count, HD)
    neighbour_values = n_values.reshape(span_count, neighbour_rows, head_count, HD)
    grad_rows = d_cross.reshape(span_count, SPAN, head_count, HD)
    scores = (
        jnp.einsum("crhd,ckhd->chrk", queries, neighbour_keys, preferred_element_type=jnp.float32)
        * scale_factor
    )
    row_max = jnp.max(scores, axis=3, keepdims=True)
    weights = jnp.exp(scores - row_max)
    probs = weights / jnp.sum(weights, axis=3, keepdims=True)
    probs_low = probs.astype(jnp.bfloat16)
    attended = jnp.einsum(
        "chrk,ckhd->crhd", probs_low, neighbour_values, preferred_element_type=jnp.float32
    )
    cross_out = attended.reshape(row_count, column_count).astype(jnp.bfloat16)
    grad_probs = jnp.einsum(
        "crhd,ckhd->chrk", grad_rows, neighbour_values, preferred_element_type=jnp.float32
    )
    centre = jnp.sum(grad_probs * probs, axis=3, keepdims=True)
    grad_scores = (probs * (grad_probs - centre) * scale_factor).astype(jnp.bfloat16)
    grad_source = jnp.einsum(
        "chrk,ckhd->crhd", grad_scores, neighbour_keys, preferred_element_type=jnp.float32
    )
    grad_source = grad_source.reshape(row_count, column_count).astype(jnp.bfloat16)
    grad_keys = jnp.einsum(
        "chrk,crhd->ckhd", grad_scores, queries, preferred_element_type=jnp.float32
    ).reshape(n_keys.shape)
    grad_values = jnp.einsum(
        "chrk,crhd->ckhd", probs_low, grad_rows, preferred_element_type=jnp.float32
    ).reshape(n_values.shape)
    carried = from_behind(grad_source[row_count - lag_rows :], ctx_count, 1)
    d_query = jnp.concatenate([carried, grad_source[: row_count - lag_rows]], axis=0)
    squares = jnp.sum(grad_keys * grad_keys) + jnp.sum(grad_values * grad_values)
    overall = squares
    for axis in ("head", "z", "outer"):
        count = lax.axis_size(axis)
        bit = 1
        while bit < count:
            overall = overall + lax.ppermute(overall, axis, [(i, i ^ bit) for i in range(count)])
            bit *= 2
    factor = lax.rsqrt(overall / element_total + 1e-06)
    d_keys = (grad_keys * factor).astype(jnp.bfloat16)
    d_values = (grad_values * factor).astype(jnp.bfloat16)
    return (cross_out, d_query, d_keys, d_values)


def solution(mesh):
    outer_count = mesh.shape["ctx"] // 8
    z_count = 8
    head_count = mesh.shape["head"]
    regrouped = Mesh(
        mesh.devices.reshape(outer_count, z_count, head_count), ("outer", "z", "head")
    )
    ctx_count = outer_count * z_count

    def body(q_self, k_self, v_self, q_cross, n_keys, n_values, d_cross):
        element_total = 2.0 * n_keys.size * ctx_count * head_count
        self_out = self_attention(q_self, k_self, v_self, outer_count, z_count)
        cross_out, d_query, d_keys, d_values = cross_attention(
            q_cross, n_keys, n_values, d_cross, ctx_count, element_total
        )
        return (self_out, cross_out, d_query, d_keys, d_values)

    spec = P(CTX, "head")
    return jax.shard_map(
        body, mesh=regrouped, in_specs=(spec,) * 7, out_specs=(spec,) * 5, check_vma=False
    )
```

```python
import math

import jax
import jax.numpy as jnp
from jax import lax
from jax.sharding import Mesh
from jax.sharding import PartitionSpec as P

HD = 128
SPAN = 64
CTX = ("outer", "z")


def from_behind(block, count, distance):
    route = [(i - distance, i) for i in range(count) if 0 <= i - distance < count]
    return lax.ppermute(block, CTX, route)


def spread(block, axis, count):
    copies = jnp.broadcast_to(block[None], (count,) + block.shape)
    return lax.all_to_all(copies, axis, 0, 0, tiled=True)


def self_attention(q_self, k_self, v_self, outer_count, z_count):
    row_count, column_count = q_self.shape
    head_count = column_count // HD
    outer_index = lax.axis_index("outer")
    z_index = lax.axis_index("z")
    pair = jnp.concatenate([k_self, v_self], axis=1)
    arrived = [pair]
    for shift in range(1, z_count):
        route = [(i, (i + shift) % z_count) for i in range(z_count)]
        arrived.append(lax.ppermute(pair, "z", route))
    group = jnp.concatenate(arrived, axis=0)
    keys = group[:, :column_count].reshape(z_count * row_count, head_count, HD)
    values = group[:, column_count:].reshape(z_count * row_count, head_count, HD)
    queries = spread(q_self, "outer", outer_count).reshape(outer_count, row_count, head_count, HD)
    sources = (z_index - jnp.arange(z_count, dtype=jnp.int32)) % z_count
    chunk_first = (outer_index * z_count + sources) * row_count
    key_positions = (
        chunk_first[:, None] + jnp.arange(row_count, dtype=jnp.int32)[None, :]
    ).reshape(z_count * row_count)
    query_starts = (jnp.arange(outer_count, dtype=jnp.int32) * z_count + z_index) * row_count
    query_positions = query_starts[:, None] + jnp.arange(row_count, dtype=jnp.int32)[None, :]
    visible = (key_positions[None, None, :] <= query_positions[:, :, None])[None]
    scores = jnp.einsum("grhd,khd->hgrk", queries, keys, preferred_element_type=jnp.float32) * (
        1.0 / math.sqrt(HD)
    )
    masked = jnp.where(visible, scores, jnp.float32(-1e30))
    part_max = jnp.max(masked, axis=3)
    weights = jnp.where(visible, jnp.exp(masked - part_max[..., None]), jnp.float32(0.0))
    part_sum = jnp.sum(weights, axis=3)
    part_acc = jnp.einsum(
        "hgrk,khd->grhd", weights.astype(jnp.bfloat16), values, preferred_element_type=jnp.float32
    )
    present = part_sum > 0
    inverse = jnp.where(present, 1.0 / jnp.where(present, part_sum, 1.0), 0.0)
    part_out = (part_acc * inverse.transpose(1, 2, 0)[..., None]).astype(jnp.bfloat16)
    level = jnp.where(present, part_max + jnp.log(jnp.where(present, part_sum, 1.0)), -1e30)
    level = level.transpose(1, 2, 0)
    pieces = []
    rest = level
    for unused in range(3):
        piece = lax.optimization_barrier(rest.astype(jnp.bfloat16))
        pieces.append(piece)
        rest = rest - piece.astype(jnp.float32)
    packed = jnp.concatenate(
        [part_out.reshape(outer_count, row_count, column_count)] + pieces, axis=2
    )
    back = lax.all_to_all(packed, "outer", 0, 0, tiled=True)
    got_out = back[:, :, :column_count].reshape(outer_count, row_count, head_count, HD)
    got_level = sum(
        back[:, :, column_count + i * head_count : column_count + (i + 1) * head_count].astype(
            jnp.float32
        )
        for i in range(3)
    )
    top = jnp.max(got_level, axis=0)
    rescale = jnp.exp(got_level - top[None])
    total = jnp.sum(rescale, axis=0)
    mixed = jnp.sum(got_out.astype(jnp.float32) * rescale[..., None], axis=0)
    out = mixed / total[..., None]
    return out.reshape(row_count, column_count).astype(jnp.bfloat16)


def cross_attention(q_cross, n_keys, n_values, d_cross, ctx_count, element_total):
    row_count, column_count = q_cross.shape
    head_count = column_count // HD
    lag_rows = SPAN - 1
    scale_factor = 1.0 / math.sqrt(HD)
    incoming = from_behind(q_cross[:lag_rows], ctx_count, -1)
    shifted = jnp.concatenate([q_cross[lag_rows:], incoming], axis=0)
    span_count = row_count // SPAN
    neighbour_rows = n_keys.shape[0] // span_count
    queries = shifted.reshape(span_count, SPAN, head_count, HD)
    neighbour_keys = n_keys.reshape(span_count, neighbour_rows, head_count, HD)
    neighbour_values = n_values.reshape(span_count, neighbour_rows, head_count, HD)
    grad_rows = d_cross.reshape(span_count, SPAN, head_count, HD)
    scores = (
        jnp.einsum("crhd,ckhd->chrk", queries, neighbour_keys, preferred_element_type=jnp.float32)
        * scale_factor
    )
    row_max = jnp.max(scores, axis=3, keepdims=True)
    weights = jnp.exp(scores - row_max)
    probs = weights / jnp.sum(weights, axis=3, keepdims=True)
    probs_low = probs.astype(jnp.bfloat16)
    attended = jnp.einsum(
        "chrk,ckhd->crhd", probs_low, neighbour_values, preferred_element_type=jnp.float32
    )
    cross_out = attended.reshape(row_count, column_count).astype(jnp.bfloat16)
    grad_probs = jnp.einsum(
        "crhd,ckhd->chrk", grad_rows, neighbour_values, preferred_element_type=jnp.float32
    )
    centre = jnp.sum(grad_probs * probs, axis=3, keepdims=True)
    grad_scores = (probs * (grad_probs - centre) * scale_factor).astype(jnp.bfloat16)
    grad_source = jnp.einsum(
        "chrk,ckhd->crhd", grad_scores, neighbour_keys, preferred_element_type=jnp.float32
    )
    grad_source = grad_source.reshape(row_count, column_count).astype(jnp.bfloat16)
    grad_keys = jnp.einsum(
        "chrk,crhd->ckhd", grad_scores, queries, preferred_element_type=jnp.float32
    ).reshape(n_keys.shape)
    grad_values = jnp.einsum(
        "chrk,crhd->ckhd", probs_low, grad_rows, preferred_element_type=jnp.float32
    ).reshape(n_values.shape)
    carried = from_behind(grad_source[row_count - lag_rows :], ctx_count, 1)
    d_query = jnp.concatenate([carried, grad_source[: row_count - lag_rows]], axis=0)
    squares = jnp.sum(grad_keys * grad_keys) + jnp.sum(grad_values * grad_values)
    device_count = ctx_count * lax.axis_size("head")
    every = lax.all_to_all(
        jnp.broadcast_to(squares[None], (device_count,)), ("outer", "z", "head"), 0, 0, tiled=True
    )
    overall = jnp.sum(every)
    factor = lax.rsqrt(overall / element_total + 1e-06)
    d_keys = (grad_keys * factor).astype(jnp.bfloat16)
    d_values = (grad_values * factor).astype(jnp.bfloat16)
    return (cross_out, d_query, d_keys, d_values)


def solution(mesh):
    outer_count = mesh.shape["ctx"] // 8
    z_count = 8
    head_count = mesh.shape["head"]
    regrouped = Mesh(
        mesh.devices.reshape(outer_count, z_count, head_count), ("outer", "z", "head")
    )
    ctx_count = outer_count * z_count

    def body(q_self, k_self, v_self, q_cross, n_keys, n_values, d_cross):
        element_total = 2.0 * n_keys.size * ctx_count * head_count
        self_out = self_attention(q_self, k_self, v_self, outer_count, z_count)
        cross_out, d_query, d_keys, d_values = cross_attention(
            q_cross, n_keys, n_values, d_cross, ctx_count, element_total
        )
        return (self_out, cross_out, d_query, d_keys, d_values)

    spec = P(CTX, "head")
    return jax.shard_map(
        body, mesh=regrouped, in_specs=(spec,) * 7, out_specs=(spec,) * 5, check_vma=False
    )
```

```python
import math

import jax
import jax.numpy as jnp
from jax import lax
from jax.sharding import Mesh
from jax.sharding import PartitionSpec as P


HD = 128
SPAN = 64
CTX = ("outer", "z")


def from_behind(block, count, distance):
    route = [(i - distance, i) for i in range(count) if 0 <= i - distance < count]
    return lax.ppermute(block, CTX, route)


def spread(block, axis, count):
    copies = jnp.broadcast_to(block[None], (count,) + block.shape)
    return lax.all_to_all(copies, axis, 0, 0, tiled=True)


def self_attention(q_self, k_self, v_self, outer_count, z_count):
    row_count, column_count = q_self.shape
    head_count = column_count // HD
    outer_index = lax.axis_index("outer")
    z_index = lax.axis_index("z")
    pair = jnp.concatenate([k_self, v_self], axis=1)
    group = spread(pair, "outer", outer_count).reshape(outer_count * row_count, 2 * column_count)
    keys = group[:, :column_count].reshape(outer_count * row_count, head_count, HD)
    values = group[:, column_count:].reshape(outer_count * row_count, head_count, HD)
    queries = spread(q_self, "z", z_count).reshape(z_count, row_count, head_count, HD)
    key_starts = (jnp.arange(outer_count, dtype=jnp.int32) * z_count + z_index) * row_count
    key_positions = (
        key_starts[:, None] + jnp.arange(row_count, dtype=jnp.int32)[None, :]
    ).reshape(outer_count * row_count)
    query_starts = (outer_index * z_count + jnp.arange(z_count, dtype=jnp.int32)) * row_count
    query_positions = query_starts[:, None] + jnp.arange(row_count, dtype=jnp.int32)[None, :]
    visible = (key_positions[None, None, :] <= query_positions[:, :, None])[None]
    scores = jnp.einsum("grhd,khd->hgrk", queries, keys, preferred_element_type=jnp.float32) * (
        1.0 / math.sqrt(HD)
    )
    masked = jnp.where(visible, scores, jnp.float32(-1e30))
    part_max = jnp.max(masked, axis=3)
    weights = jnp.where(visible, jnp.exp(masked - part_max[..., None]), jnp.float32(0.0))
    part_sum = jnp.sum(weights, axis=3)
    part_acc = jnp.einsum(
        "hgrk,khd->grhd", weights.astype(jnp.bfloat16), values, preferred_element_type=jnp.float32
    )
    present = part_sum > 0
    inverse = jnp.where(present, 1.0 / jnp.where(present, part_sum, 1.0), 0.0)
    part_out = (part_acc * inverse.transpose(1, 2, 0)[..., None]).astype(jnp.bfloat16)
    level = jnp.where(present, part_max + jnp.log(jnp.where(present, part_sum, 1.0)), -1e30)
    level = level.transpose(1, 2, 0)
    pieces = []
    rest = level
    for _ in range(3):
        piece = lax.optimization_barrier(rest.astype(jnp.bfloat16))
        pieces.append(piece)
        rest = rest - piece.astype(jnp.float32)
    packed = jnp.concatenate(
        [part_out.reshape(z_count, row_count, column_count)] + pieces, axis=2
    )
    back = lax.all_to_all(packed, "z", 0, 0, tiled=True)
    got_out = back[:, :, :column_count].reshape(z_count, row_count, head_count, HD)
    got_level = sum(
        back[:, :, column_count + i * head_count : column_count + (i + 1) * head_count].astype(
            jnp.float32
        )
        for i in range(3)
    )
    top = jnp.max(got_level, axis=0)
    rescale = jnp.exp(got_level - top[None])
    total = jnp.sum(rescale, axis=0)
    mixed = jnp.sum(got_out.astype(jnp.float32) * rescale[..., None], axis=0)
    out = mixed / total[..., None]
    return out.reshape(row_count, column_count).astype(jnp.bfloat16)


def cross_attention(q_cross, n_keys, n_values, d_cross, ctx_count, element_total):
    row_count, column_count = q_cross.shape
    head_count = column_count // HD
    lag_rows = SPAN - 1
    scale_factor = 1.0 / math.sqrt(HD)
    incoming = from_behind(q_cross[:lag_rows], ctx_count, -1)
    shifted = jnp.concatenate([q_cross[lag_rows:], incoming], axis=0)
    span_count = row_count // SPAN
    neighbour_rows = n_keys.shape[0] // span_count
    queries = shifted.reshape(span_count, SPAN, head_count, HD)
    neighbour_keys = n_keys.reshape(span_count, neighbour_rows, head_count, HD)
    neighbour_values = n_values.reshape(span_count, neighbour_rows, head_count, HD)
    grad_rows = d_cross.reshape(span_count, SPAN, head_count, HD)
    scores = (
        jnp.einsum("crhd,ckhd->chrk", queries, neighbour_keys, preferred_element_type=jnp.float32)
        * scale_factor
    )
    row_max = jnp.max(scores, axis=3, keepdims=True)
    weights = jnp.exp(scores - row_max)
    probs = weights / jnp.sum(weights, axis=3, keepdims=True)
    probs_low = probs.astype(jnp.bfloat16)
    attended = jnp.einsum(
        "chrk,ckhd->crhd", probs_low, neighbour_values, preferred_element_type=jnp.float32
    )
    cross_out = attended.reshape(row_count, column_count).astype(jnp.bfloat16)
    grad_probs = jnp.einsum(
        "crhd,ckhd->chrk", grad_rows, neighbour_values, preferred_element_type=jnp.float32
    )
    centre = jnp.sum(grad_probs * probs, axis=3, keepdims=True)
    grad_scores = (probs * (grad_probs - centre) * scale_factor).astype(jnp.bfloat16)
    grad_source = jnp.einsum(
        "chrk,ckhd->crhd", grad_scores, neighbour_keys, preferred_element_type=jnp.float32
    )
    grad_source = grad_source.reshape(row_count, column_count).astype(jnp.bfloat16)
    grad_keys = jnp.einsum(
        "chrk,crhd->ckhd", grad_scores, queries, preferred_element_type=jnp.float32
    ).reshape(n_keys.shape)
    grad_values = jnp.einsum(
        "chrk,crhd->ckhd", probs_low, grad_rows, preferred_element_type=jnp.float32
    ).reshape(n_values.shape)
    carried = from_behind(grad_source[row_count - lag_rows :], ctx_count, 1)
    d_query = jnp.concatenate([carried, grad_source[: row_count - lag_rows]], axis=0)
    squares = jnp.sum(grad_keys * grad_keys) + jnp.sum(grad_values * grad_values)
    device_count = ctx_count * lax.axis_size("head")
    every = lax.all_to_all(
        jnp.broadcast_to(squares[None], (device_count,)), ("outer", "z", "head"), 0, 0, tiled=True
    )
    overall = jnp.sum(every)
    factor = lax.rsqrt(overall / element_total + 1e-06)
    d_keys = (grad_keys * factor).astype(jnp.bfloat16)
    d_values = (grad_values * factor).astype(jnp.bfloat16)
    return (cross_out, d_query, d_keys, d_values)


def solution(mesh):
    outer_count = mesh.shape["ctx"] // 8
    z_count = 8
    head_count = mesh.shape["head"]
    regrouped = Mesh(
        mesh.devices.reshape(outer_count, z_count, head_count), ("outer", "z", "head")
    )
    ctx_count = outer_count * z_count

    def body(q_self, k_self, v_self, q_cross, n_keys, n_values, d_cross):
        element_total = 2.0 * n_keys.size * ctx_count * head_count
        self_out = self_attention(q_self, k_self, v_self, outer_count, z_count)
        cross_out, d_query, d_keys, d_values = cross_attention(
            q_cross, n_keys, n_values, d_cross, ctx_count, element_total
        )
        return (self_out, cross_out, d_query, d_keys, d_values)

    spec = P(CTX, "head")
    return jax.shard_map(
        body, mesh=regrouped, in_specs=(spec,) * 7, out_specs=(spec,) * 5, check_vma=False
    )
```

```python
import math

import jax
import jax.numpy as jnp
from jax import lax
from jax.sharding import Mesh
from jax.sharding import PartitionSpec as P


HD = 128
SPAN = 64
CTX = ("outer", "z")


def from_behind(block, count, distance):
    route = [(i - distance, i) for i in range(count) if 0 <= i - distance < count]
    return lax.ppermute(block, CTX, route)


def spread(block, axis, count):
    copies = jnp.broadcast_to(block[None], (count,) + block.shape)
    return lax.all_to_all(copies, axis, 0, 0, tiled=True)


def self_attention(q_self, k_self, v_self, outer_count, z_count):
    row_count, column_count = q_self.shape
    head_count = column_count // HD
    outer_index = lax.axis_index("outer")
    z_index = lax.axis_index("z")
    pair = jnp.concatenate([k_self, v_self], axis=1)
    group = spread(pair, "z", z_count).reshape(z_count * row_count, 2 * column_count)
    keys = group[:, :column_count].reshape(z_count * row_count, head_count, HD)
    values = group[:, column_count:].reshape(z_count * row_count, head_count, HD)
    queries = spread(q_self, "outer", outer_count).reshape(outer_count, row_count, head_count, HD)
    key_first = outer_index * z_count * row_count
    key_positions = key_first + jnp.arange(z_count * row_count, dtype=jnp.int32)
    query_starts = (jnp.arange(outer_count, dtype=jnp.int32) * z_count + z_index) * row_count
    query_positions = query_starts[:, None] + jnp.arange(row_count, dtype=jnp.int32)[None, :]
    visible = (key_positions[None, None, :] <= query_positions[:, :, None])[None]
    scores = jnp.einsum("grhd,khd->hgrk", queries, keys, preferred_element_type=jnp.float32) * (
        1.0 / math.sqrt(HD)
    )
    masked = jnp.where(visible, scores, jnp.float32(-1e30))
    part_max = jnp.max(masked, axis=3)
    weights = jnp.where(visible, jnp.exp(masked - part_max[..., None]), jnp.float32(0.0))
    part_sum = jnp.sum(weights, axis=3)
    part_acc = jnp.einsum(
        "hgrk,khd->grhd", weights.astype(jnp.bfloat16), values, preferred_element_type=jnp.float32
    )
    present = part_sum > 0
    inverse = jnp.where(present, 1.0 / jnp.where(present, part_sum, 1.0), 0.0)
    part_out = (part_acc * inverse.transpose(1, 2, 0)[..., None]).astype(jnp.bfloat16)
    level = jnp.where(present, part_max + jnp.log(jnp.where(present, part_sum, 1.0)), -1e30)
    level = level.transpose(1, 2, 0)
    pieces = []
    rest = level
    for _ in range(3):
        piece = lax.optimization_barrier(rest.astype(jnp.bfloat16))
        pieces.append(piece)
        rest = rest - piece.astype(jnp.float32)
    stat_rows = jnp.concatenate(pieces, axis=2).reshape(outer_count, -1, column_count)
    packed = jnp.concatenate(
        [part_out.reshape(outer_count, row_count, column_count), stat_rows], axis=1
    )
    back = lax.all_to_all(packed, "outer", 0, 0, tiled=True)
    got_out = back[:, :row_count].reshape(outer_count, row_count, head_count, HD)
    got_stats = back[:, row_count:].reshape(outer_count, row_count, 3 * head_count)
    got_level = sum(
        got_stats[:, :, i * head_count : (i + 1) * head_count].astype(jnp.float32)
        for i in range(3)
    )
    top = jnp.max(got_level, axis=0)
    rescale = jnp.exp(got_level - top[None])
    total = jnp.sum(rescale, axis=0)
    mixed = jnp.sum(got_out.astype(jnp.float32) * rescale[..., None], axis=0)
    out = mixed / total[..., None]
    return out.reshape(row_count, column_count).astype(jnp.bfloat16)


def cross_attention(q_cross, n_keys, n_values, d_cross, ctx_count, element_total):
    row_count, column_count = q_cross.shape
    head_count = column_count // HD
    lag_rows = SPAN - 1
    scale_factor = 1.0 / math.sqrt(HD)
    incoming = from_behind(q_cross[:lag_rows], ctx_count, -1)
    shifted = jnp.concatenate([q_cross[lag_rows:], incoming], axis=0)
    span_count = row_count // SPAN
    neighbour_rows = n_keys.shape[0] // span_count
    queries = shifted.reshape(span_count, SPAN, head_count, HD)
    neighbour_keys = n_keys.reshape(span_count, neighbour_rows, head_count, HD)
    neighbour_values = n_values.reshape(span_count, neighbour_rows, head_count, HD)
    grad_rows = d_cross.reshape(span_count, SPAN, head_count, HD)
    scores = (
        jnp.einsum("crhd,ckhd->chrk", queries, neighbour_keys, preferred_element_type=jnp.float32)
        * scale_factor
    )
    row_max = jnp.max(scores, axis=3, keepdims=True)
    weights = jnp.exp(scores - row_max)
    probs = weights / jnp.sum(weights, axis=3, keepdims=True)
    probs_low = probs.astype(jnp.bfloat16)
    attended = jnp.einsum(
        "chrk,ckhd->crhd", probs_low, neighbour_values, preferred_element_type=jnp.float32
    )
    cross_out = attended.reshape(row_count, column_count).astype(jnp.bfloat16)
    grad_probs = jnp.einsum(
        "crhd,ckhd->chrk", grad_rows, neighbour_values, preferred_element_type=jnp.float32
    )
    centre = jnp.sum(grad_probs * probs, axis=3, keepdims=True)
    grad_scores = (probs * (grad_probs - centre) * scale_factor).astype(jnp.bfloat16)
    grad_source = jnp.einsum(
        "chrk,ckhd->crhd", grad_scores, neighbour_keys, preferred_element_type=jnp.float32
    )
    grad_source = grad_source.reshape(row_count, column_count).astype(jnp.bfloat16)
    grad_keys = jnp.einsum(
        "chrk,crhd->ckhd", grad_scores, queries, preferred_element_type=jnp.float32
    ).reshape(n_keys.shape)
    grad_values = jnp.einsum(
        "chrk,crhd->ckhd", probs_low, grad_rows, preferred_element_type=jnp.float32
    ).reshape(n_values.shape)
    carried = from_behind(grad_source[row_count - lag_rows :], ctx_count, 1)
    d_query = jnp.concatenate([carried, grad_source[: row_count - lag_rows]], axis=0)
    squares = jnp.sum(grad_keys * grad_keys) + jnp.sum(grad_values * grad_values)
    device_count = ctx_count * lax.axis_size("head")
    every = lax.all_to_all(
        jnp.broadcast_to(squares[None], (device_count,)), ("outer", "z", "head"), 0, 0, tiled=True
    )
    overall = jnp.sum(every)
    factor = lax.rsqrt(overall / element_total + 1e-06)
    d_keys = (grad_keys * factor).astype(jnp.bfloat16)
    d_values = (grad_values * factor).astype(jnp.bfloat16)
    return (cross_out, d_query, d_keys, d_values)


def solution(mesh):
    outer_count = mesh.shape["ctx"] // 8
    z_count = 8
    head_count = mesh.shape["head"]
    regrouped = Mesh(
        mesh.devices.reshape(outer_count, z_count, head_count), ("outer", "z", "head")
    )
    ctx_count = outer_count * z_count

    def body(q_self, k_self, v_self, q_cross, n_keys, n_values, d_cross):
        element_total = 2.0 * n_keys.size * ctx_count * head_count
        self_out = self_attention(q_self, k_self, v_self, outer_count, z_count)
        cross_out, d_query, d_keys, d_values = cross_attention(
            q_cross, n_keys, n_values, d_cross, ctx_count, element_total
        )
        return (self_out, cross_out, d_query, d_keys, d_values)

    spec = P(CTX, "head")
    return jax.shard_map(
        body, mesh=regrouped, in_specs=(spec,) * 7, out_specs=(spec,) * 5, check_vma=False
    )
```
